256 devices in a mesh: space: 32 (over z, x), mode: 8 (over y, core).
Axes of the slice: x: 4, y: 4, z: 8, core: 2. Of those that a mesh axis runs over, the one named last changes fastest.
Arguments:
- vectors: float32 [55296, 256], P('space', 'mode'), may hold values from -6 to 6
- force_blocks: float32 [288, 27, 192, 192], P('space', None, 'mode'), as said below
- inverse_blocks: float32 [288, 192, 192], P('space'), as said below
- neighbours: int32 [288, 27], P('space'), may hold values from 0 to 287, as said below
Outputs:
- w_block: float32 [55296, 256], P('space', 'mode')
- hw_block: float32 [55296, 256], P('space', 'mode')
- gram_a: float32 [512, 2, 256], P(None, None, 'mode')
- gram_b: float32 [512, 2, 256], P(None, None, 'mode')
The draws below stay inside these ranges and needn't reach their ends.
Inputs may be any that keep to these rules, and one draw needn't show every extreme that they name: `neighbours`: block rows are atom cells on a periodic grid of 32 layers of 3 x 3 cells; the rows of layer z are z * 9 to z * 9 + 8 in some order. Entry k = 9 (dz + 1) + 3 (dy + 1) + (dx + 1) of row i is the block row of the cell at offset (dz, dy, dx) from row i's cell, so entry 13 is i itself. H is symmetric: force_blocks[neighbours[i, k], 26 - k] is the transpose of force_blocks[i, k]. `inverse_blocks`: every block is symmetric.
All inputs are finite; a program needn't handle non-finite values.
Results may differ from the reference program's by a relative error of at most 0.00013.
Values sent between devices are 32-bit elements; how exact they have to be, the bound alone decides.
No kernel may reach another device: no remote copies, remote signals or barrier semaphores. Data moves between devices by JAX's collectives and lax.ppermute only.
A program may use at most 128 MiB of HBM per device.

```python
import math
import jax
import jax.numpy as jnp
from jax import lax

BLOCK = 192
MODES = 256
NEIGH = 27
CELLS = 9
NB = 288
NROWS = 55296


def permute_layer(layer_key):
    return jax.random.permutation(layer_key, CELLS)


def neighbour_lists(key):
    layer_count = NB // CELLS
    key_list = jax.random.split(jax.random.fold_in(key, 1), layer_count)
    layer_perms = jax.vmap(permute_layer)(key_list).astype(jnp.int32)
    position_of = jnp.argsort(layer_perms, axis=1, stable=True).astype(jnp.int32)
    row_ids = jnp.arange(NB, dtype=jnp.int32)
    layer_index = row_ids // CELLS
    position = row_ids % CELLS
    cell_index = layer_perms[layer_index, position]
    cell_x = cell_index // 3
    cell_y = cell_index % 3
    offsets = jnp.arange(NEIGH, dtype=jnp.int32)
    shift_z = offsets // 9 - 1
    shift_y = offsets // 3 % 3 - 1
    shift_x = offsets % 3 - 1
    near_layer = (layer_index[:, None] + shift_z[None, :]) % layer_count
    near_x = (cell_x[:, None] + shift_x[None, :]) % 3
    near_y = (cell_y[:, None] + shift_y[None, :]) % 3
    result = near_layer * CELLS + position_of[near_layer, near_x * 3 + near_y]
    return result.astype(jnp.int32)


def draw_neighbours(key, part):
    return neighbour_lists(key)


def draw_force_blocks(key, part):
    lists = neighbour_lists(key)
    noise_key, centre_key, shift_key = jax.random.split(jax.random.fold_in(key, 7), 3)
    lower_dims = (NB, 13, BLOCK, BLOCK)
    centre_dims = (NB, BLOCK, BLOCK)
    base = jax.random.normal(noise_key, lower_dims, jnp.float32)
    centre_noise = jax.random.normal(centre_key, centre_dims, jnp.float32)
    upper_end = 10.0
    factor = 1.0 / math.sqrt(NEIGH * BLOCK)
    base = base * factor
    centre_noise = 0.5 * (centre_noise + jnp.swapaxes(centre_noise, 1, 2)) * factor * math.sqrt(2.0)
    upper_offsets = jnp.arange(14, NEIGH, dtype=jnp.int32)
    mirror_offsets = (26 - upper_offsets).astype(jnp.int32)
    mirrored = base[lists[:, 14:], mirror_offsets[None, :]]
    mirrored = jnp.swapaxes(mirrored, 2, 3)
    spread = jax.random.uniform(shift_key, (NB, BLOCK), jnp.float32)
    shifts = jnp.exp(spread * math.log(upper_end))
    layer_index = (jnp.arange(NB) // CELLS).astype(jnp.float32)
    growth = 1.0 + 2.0 * layer_index / (NB // CELLS - 1)
    shifts = shifts * growth[:, None]
    identity = jnp.eye(BLOCK, dtype=jnp.float32)
    centre = centre_noise + identity[None] * shifts[:, :, None]
    return jnp.concatenate([base, centre[:, None], mirrored], axis=1)


def draw_inverse_blocks(key, part):
    noise_key, diag_key = jax.random.split(jax.random.fold_in(key, 11))
    dims_all = (NB, BLOCK, BLOCK)
    noise = jax.random.normal(noise_key, dims_all, jnp.float32)
    noise = 0.5 * (noise + jnp.swapaxes(noise, 1, 2)) * (0.5 * math.sqrt(2.0) / math.sqrt(BLOCK))
    spread = jax.random.uniform(diag_key, (NB, BLOCK), jnp.float32)
    diagonal = 0.2 * jnp.exp(spread * math.log(5.0))
    identity = jnp.eye(BLOCK, dtype=jnp.float32)
    return noise + identity[None] * diagonal[:, :, None]


def block_levels(rng, shape, pieces, least, high):
    level, own = 1.0, jax.random.fold_in(rng, 6)
    for axis_at, parts in pieces:
        steps = jnp.exp(jax.random.uniform(jax.random.fold_in(own, axis_at), (parts,), jnp.float32, least / len(pieces), high / len(pieces)))
        level = level * jnp.repeat(steps, shape[axis_at] // parts).reshape([-1 if axis == axis_at else 1 for axis in range(len(shape))])
    return level


def bell_draw(stream_key, extent, deviation, bound, shards=(), kind=jnp.bfloat16):
    loudness = block_levels(stream_key, extent, shards, -0.22, 0.18) if shards else 1.0
    entries = jax.random.normal(stream_key, extent, jnp.float32) * deviation * loudness
    return jnp.minimum(jnp.maximum(entries, -bound), bound).astype(kind)


def setup_inputs(seed: int = 0) -> dict:
    keys = jax.random.split(jax.random.key(seed), 5)
    return {
        "vectors": bell_draw(keys[0], (NROWS, MODES), 1.0, 6.0, ((0, 32), (1, 8)), jnp.float32),
        "force_blocks": draw_force_blocks(jax.random.fold_in(keys[4], 71), 0),
        "inverse_blocks": draw_inverse_blocks(jax.random.fold_in(keys[4], 71), 0),
        "neighbours": draw_neighbours(jax.random.fold_in(keys[4], 71), 0),
    }


def apply_force(force_blocks, neighbours, block_field):

    def accumulate(totals, offset):
        gathered = jnp.take(block_field, neighbours[:, offset], axis=0)
        force_slice = lax.dynamic_index_in_dim(force_blocks, offset, 1, keepdims=False)
        product = jnp.einsum('brc,bcm->brm', force_slice, gathered, precision=lax.Precision.HIGHEST, preferred_element_type=jnp.float32)
        return (totals + product, None)
    initial = jnp.zeros(block_field.shape, jnp.float32)
    totals, unused = lax.scan(accumulate, initial, jnp.arange(NEIGH, dtype=jnp.int32))
    return totals

def reference(vectors, force_blocks, inverse_blocks, neighbours):
    stacked_x = vectors.reshape(NB, BLOCK, MODES)
    image_x = apply_force(force_blocks, neighbours, stacked_x).reshape(NROWS, MODES)
    rayleigh = jnp.dot(vectors.T, image_x, precision=lax.Precision.HIGHEST, preferred_element_type=jnp.float32) / NROWS
    residual = image_x - jnp.dot(vectors, rayleigh, precision=lax.Precision.HIGHEST, preferred_element_type=jnp.float32)
    search_raw = jnp.einsum('brc,bcm->brm', inverse_blocks, residual.reshape(NB, BLOCK, MODES), precision=lax.Precision.HIGHEST, preferred_element_type=jnp.float32).reshape(NROWS, MODES)
    scales = lax.rsqrt(lax.optimization_barrier(jnp.mean(search_raw * search_raw, axis=0)) + 1e-06)
    w_block = search_raw * scales
    hw_block = apply_force(force_blocks, neighbours, w_block.reshape(NB, BLOCK, MODES)).reshape(NROWS, MODES)
    basis = jnp.concatenate([vectors, w_block], axis=1)
    columns_b = jnp.stack([vectors, w_block], axis=1)
    columns_a = jnp.stack([image_x, hw_block], axis=1)
    gram_a = jnp.einsum('ra,rgj->agj', basis, columns_a, precision=lax.Precision.HIGHEST, preferred_element_type=jnp.float32) / NROWS
    gram_b = jnp.einsum('ra,rgj->agj', basis, columns_b, precision=lax.Precision.HIGHEST, preferred_element_type=jnp.float32) / NROWS
    return (w_block, hw_block, gram_a, gram_b)
```

```python
import jax
import jax.numpy as jnp
from jax import lax
from jax.sharding import PartitionSpec as P

CELLS = 9
HIGHEST = lax.Precision.HIGHEST


def space_sum(value):
    count = lax.axis_size("space")
    step = 1
    while step < count:
        pairs = [(i, i ^ step) for i in range(count)]
        value = value + lax.ppermute(value, "space", pairs)
        step *= 2
    return value


def halo(block, width):
    count = lax.axis_size("space")
    forward = [(i, (i + 1) % count) for i in range(count)]
    backward = [((i + 1) % count, i) for i in range(count)]
    low = lax.ppermute(block[block.shape[0] - width :], "space", forward)
    high = lax.ppermute(block[:width], "space", backward)
    return low, high


def dense_rows(force_blocks, local_ids, ext_blocks):
    block_rows, neigh = local_ids.shape
    columns = jnp.arange(ext_blocks, dtype=jnp.int32)
    onehot = local_ids[:, :, None] == columns[None, None, :]
    offsets = jnp.arange(neigh, dtype=jnp.int32)
    which = jnp.sum(jnp.where(onehot, offsets[None, :, None], 0), axis=1)
    valid = jnp.any(onehot, axis=1)
    flat = (jnp.arange(block_rows, dtype=jnp.int32)[:, None] * neigh + which).reshape(-1)
    rows, cols = force_blocks.shape[2], force_blocks.shape[3]
    table = force_blocks.reshape(block_rows * neigh, rows * cols)
    picked = jnp.take(table, flat, axis=0).reshape(block_rows, ext_blocks, rows, cols)
    return jnp.where(valid[:, :, None, None], picked, 0.0)


def apply_dense(dense, low, own, high):
    width = low.shape[0]
    own_count = own.shape[0]
    parts = (
        (dense[:, width : width + own_count], own),
        (dense[:, :width], low),
        (dense[:, width + own_count :], high),
    )
    total = None
    for coeffs, field in parts:
        product = jnp.einsum(
            "ijrc,jcm->irm",
            coeffs,
            field,
            precision=HIGHEST,
            preferred_element_type=jnp.float32,
        )
        total = product if total is None else total + product
    regrouped = lax.all_to_all(total, "mode", split_axis=2, concat_axis=1, tiled=True)
    return regrouped.reshape(-1, regrouped.shape[2])


def local(vectors, force_blocks, inverse_blocks, neighbours):
    row_count, col_count = vectors.shape
    block_size = inverse_blocks.shape[1]
    block_rows = row_count // block_size
    slab_count = lax.axis_size("space")
    total_rows = row_count * slab_count
    own_layers = block_rows // CELLS
    layer_total = own_layers * slab_count
    slab_index = lax.axis_index("space")
    mode_index = lax.axis_index("mode")
    layer_of = neighbours // CELLS
    relative = (layer_of - slab_index * own_layers + 1) % layer_total
    local_ids = relative * CELLS + neighbours % CELLS
    ext_blocks = block_rows + 2 * CELLS
    dense = dense_rows(force_blocks, local_ids, ext_blocks)

    stacked_x = vectors.reshape(block_rows, block_size, col_count)
    full_x = lax.all_gather(stacked_x, "mode", axis=2, tiled=True)
    low_x, high_x = halo(full_x, CELLS)
    image_x = apply_dense(dense, low_x, full_x, high_x)
    mode_count = full_x.shape[2]
    flat_x = full_x.reshape(row_count, mode_count)
    rayleigh = (
        space_sum(
            jnp.einsum(
                "ra,rj->aj",
                flat_x,
                image_x,
                precision=HIGHEST,
                preferred_element_type=jnp.float32,
            )
        )
        / total_rows
    )
    residual = image_x - jnp.dot(
        flat_x, rayleigh, precision=HIGHEST, preferred_element_type=jnp.float32
    )
    search_raw = jnp.einsum(
        "brc,bcm->brm",
        inverse_blocks,
        residual.reshape(block_rows, block_size, col_count),
        precision=HIGHEST,
        preferred_element_type=jnp.float32,
    )
    full_s = lax.all_gather(search_raw, "mode", axis=2, tiled=True)
    low_s, high_s = halo(full_s, CELLS)
    image_s = apply_dense(dense, low_s, full_s, high_s)
    flat_s = full_s.reshape(row_count, mode_count)
    own_s = search_raw.reshape(row_count, col_count)

    squares = jnp.sum(flat_s * flat_s, axis=0)
    basis = jnp.concatenate([flat_x, flat_s], axis=1)
    columns = jnp.stack([vectors, own_s, image_x, image_s], axis=1)
    gram_part = jnp.einsum(
        "ra,rgj->agj", basis, columns, precision=HIGHEST, preferred_element_type=jnp.float32
    )
    packed = jnp.concatenate([gram_part.reshape(-1), squares])
    summed = space_sum(packed)
    gram_sum = summed[: gram_part.size].reshape(gram_part.shape)
    scales_all = lax.rsqrt(summed[gram_part.size :] / total_rows + 1e-06)
    scales_own = lax.dynamic_slice_in_dim(scales_all, mode_index * col_count, col_count)

    w_block = own_s * scales_own
    hw_block = image_s * scales_own
    row_scale = jnp.concatenate([jnp.ones((mode_count,), jnp.float32), scales_all])
    ones_own = jnp.ones((col_count,), jnp.float32)
    col_scale = jnp.stack([ones_own, scales_own, ones_own, scales_own])
    gram = gram_sum * row_scale[:, None, None] * col_scale[None] / total_rows
    gram_b = gram[:, 0:2]
    gram_a = gram[:, 2:4]
    return (w_block, hw_block, gram_a, gram_b)


def solution(mesh):
    in_specs = (
        P("space", "mode"),
        P("space", None, "mode", None),
        P("space", None, None),
        P("space", None),
    )
    out_specs = (
        P("space", "mode"),
        P("space", "mode"),
        P(None, None, "mode"),
        P(None, None, "mode"),
    )
    return jax.shard_map(local, mesh=mesh, in_specs=in_specs, out_specs=out_specs, check_vma=False)
```

```python
import jax
import jax.numpy as jnp
from jax import lax
from jax.sharding import PartitionSpec as P

CELLS = 9
HIGHEST = lax.Precision.HIGHEST


def space_sum(value):
    count = lax.axis_size("space")
    step = 1
    while step < count:
        pairs = [(i, i ^ step) for i in range(count)]
        value = value + lax.ppermute(value, "space", pairs)
        step *= 2
    return value


def halo(block, width):
    count = lax.axis_size("space")
    forward = [(i, (i + 1) % count) for i in range(count)]
    backward = [((i + 1) % count, i) for i in range(count)]
    mode_count = lax.axis_size("mode")
    core = lax.axis_index("mode") % 2
    half = block.shape[2] // 2
    siblings = [(i, i ^ 1) for i in range(mode_count)]

    def send(piece, pairs):
        mine = lax.dynamic_slice_in_dim(piece, core * half, half, axis=2)
        got = lax.ppermute(mine, "space", pairs)
        other = lax.ppermute(got, "mode", siblings)
        return jnp.where(
            core == 0,
            jnp.concatenate([got, other], axis=2),
            jnp.concatenate([other, got], axis=2),
        )

    low = send(block[block.shape[0] - width :], forward)
    high = send(block[:width], backward)
    return low, high


def dense_rows(force_blocks, local_ids, ext_blocks):
    block_rows, neigh = local_ids.shape
    columns = jnp.arange(ext_blocks, dtype=jnp.int32)
    onehot = local_ids[:, :, None] == columns[None, None, :]
    rows, cols = force_blocks.shape[2], force_blocks.shape[3]
    table = force_blocks.reshape(block_rows, neigh, rows * cols)
    picked = jnp.einsum(
        "ikj,ikx->ijx",
        onehot.astype(jnp.float32),
        table,
        precision=HIGHEST,
        preferred_element_type=jnp.float32,
    )
    return picked.reshape(block_rows, ext_blocks, rows, cols)


def apply_dense(dense, low, own, high):
    width = low.shape[0]
    own_count = own.shape[0]
    mode_count = lax.axis_size("mode")

    def split(field):
        return field.reshape(field.shape[0], field.shape[1], mode_count, -1)

    parts = (
        (dense[:, width : width + own_count], own),
        (dense[:, :width], low),
        (dense[:, width + own_count :], high),
    )
    total = None
    for coeffs, field in parts:
        product = jnp.einsum(
            "ijrc,jcdm->dirm",
            coeffs,
            split(field),
            precision=HIGHEST,
            preferred_element_type=jnp.float32,
        )
        total = product if total is None else total + product
    regrouped = lax.all_to_all(total, "mode", split_axis=0, concat_axis=0, tiled=True)
    regrouped = jnp.transpose(regrouped, (1, 0, 2, 3))
    return regrouped.reshape(-1, regrouped.shape[3])


def local(vectors, force_blocks, inverse_blocks, neighbours):
    row_count, col_count = vectors.shape
    block_size = inverse_blocks.shape[1]
    block_rows = row_count // block_size
    slab_count = lax.axis_size("space")
    total_rows = row_count * slab_count
    own_layers = block_rows // CELLS
    layer_total = own_layers * slab_count
    slab_index = lax.axis_index("space")
    mode_index = lax.axis_index("mode")
    layer_of = neighbours // CELLS
    relative = (layer_of - slab_index * own_layers + 1) % layer_total
    local_ids = relative * CELLS + neighbours % CELLS
    ext_blocks = block_rows + 2 * CELLS
    dense = dense_rows(force_blocks, local_ids, ext_blocks)

    stacked_x = vectors.reshape(block_rows, block_size, col_count)
    full_x = lax.all_gather(stacked_x, "mode", axis=2, tiled=True)
    low_x, high_x = halo(full_x, CELLS)
    image_x = apply_dense(dense, low_x, full_x, high_x)
    mode_count = full_x.shape[2]
    flat_x = full_x.reshape(row_count, mode_count)
    rayleigh = (
        space_sum(
            jnp.einsum(
                "ra,rj->aj",
                flat_x,
                image_x,
                precision=HIGHEST,
                preferred_element_type=jnp.float32,
            )
        )
        / total_rows
    )
    residual = image_x - jnp.dot(
        flat_x, rayleigh, precision=HIGHEST, preferred_element_type=jnp.float32
    )
    search_raw = jnp.einsum(
        "brc,bcm->brm",
        inverse_blocks,
        residual.reshape(block_rows, block_size, col_count),
        precision=HIGHEST,
        preferred_element_type=jnp.float32,
    )
    full_s = lax.all_gather(search_raw, "mode", axis=2, tiled=True)
    flat_s = full_s.reshape(row_count, mode_count)
    own_s = search_raw.reshape(row_count, col_count)

    squares = jnp.sum(flat_s * flat_s, axis=0)
    cross = jnp.einsum(
        "ra,rgj->agj",
        flat_s,
        jnp.stack([vectors, own_s, image_x], axis=1),
        precision=HIGHEST,
        preferred_element_type=jnp.float32,
    )
    x_s = jnp.einsum(
        "ra,rgj->agj",
        flat_x,
        jnp.stack([vectors, own_s], axis=1),
        precision=HIGHEST,
        preferred_element_type=jnp.float32,
    )
    packed = jnp.concatenate([cross.reshape(-1), x_s.reshape(-1), squares])
    summed = space_sum(packed)
    cross_sum = summed[: cross.size].reshape(cross.shape)
    x_s_sum = summed[cross.size : cross.size + x_s.size].reshape(x_s.shape)
    scales_all = lax.rsqrt(summed[cross.size + x_s.size :] / total_rows + 1e-06)
    scales_own = lax.dynamic_slice_in_dim(scales_all, mode_index * col_count, col_count)

    low_s, high_s = halo(full_s, CELLS)
    image_s = apply_dense(dense, low_s, full_s, high_s)
    basis = jnp.concatenate([flat_x, flat_s], axis=1)
    last = space_sum(
        jnp.einsum(
            "ra,rj->aj", basis, image_s, precision=HIGHEST, preferred_element_type=jnp.float32
        )
    )

    w_block = own_s * scales_own
    hw_block = image_s * scales_own
    col = scales_own[None, :]
    row = scales_all[:, None]
    gram_b = jnp.concatenate(
        [
            jnp.stack([x_s_sum[:, 0], x_s_sum[:, 1] * col], axis=1) / total_rows,
            jnp.stack([cross_sum[:, 0] * row, cross_sum[:, 1] * row * col], axis=1) / total_rows,
        ],
        axis=0,
    )
    gram_a = jnp.concatenate(
        [
            jnp.stack([rayleigh, last[:mode_count] * col / total_rows], axis=1),
            jnp.stack([cross_sum[:, 2] * row, last[mode_count:] * row * col], axis=1) / total_rows,
        ],
        axis=0,
    )
    return (w_block, hw_block, gram_a, gram_b)


def solution(mesh):
    in_specs = (
        P("space", "mode"),
        P("space", None, "mode", None),
        P("space", None, None),
        P("space", None),
    )
    out_specs = (
        P("space", "mode"),
        P("space", "mode"),
        P(None, None, "mode"),
        P(None, None, "mode"),
    )
    return jax.shard_map(local, mesh=mesh, in_specs=in_specs, out_specs=out_specs, check_vma=False)
```

```python
import jax
import jax.numpy as jnp
from jax import lax
from jax.sharding import PartitionSpec as P


CELLS = 9
HIGHEST = lax.Precision.HIGHEST


def space_sum(value):
    count = lax.axis_size("space")
    step = 1
    while step < count:
        pairs = [(i, i ^ step) for i in range(count)]
        value = value + lax.ppermute(value, "space", pairs)
        step *= 2
    return value


def halo(block, width):
    count = lax.axis_size("space")
    forward = [(i, (i + 1) % count) for i in range(count)]
    backward = [((i + 1) % count, i) for i in range(count)]
    mode_count = lax.axis_size("mode")
    core = lax.axis_index("mode") % 2
    half = block.shape[2] // 2
    siblings = [(i, i ^ 1) for i in range(mode_count)]

    def send(piece, pairs):
        mine = lax.dynamic_slice_in_dim(piece, core * half, half, axis=2)
        got = lax.ppermute(mine, "space", pairs)
        other = lax.ppermute(got, "mode", siblings)
        return jnp.where(
            core == 0,
            jnp.concatenate([got, other], axis=2),
            jnp.concatenate([other, got], axis=2),
        )

    low = send(block[block.shape[0] - width :], forward)
    high = send(block[:width], backward)
    return low, high


def dense_rows(force_blocks, local_ids, ext_blocks):
    block_rows, neigh = local_ids.shape
    columns = jnp.arange(ext_blocks, dtype=jnp.int32)
    onehot = local_ids[:, :, None] == columns[None, None, :]
    offsets = jnp.arange(neigh, dtype=jnp.int32)
    which = jnp.sum(jnp.where(onehot, offsets[None, :, None], 0), axis=1)
    valid = jnp.any(onehot, axis=1)
    picked = force_blocks[jnp.arange(block_rows, dtype=jnp.int32)[:, None], which]
    return jnp.where(valid[:, :, None, None], picked, 0.0)


def apply_dense(dense, low, own, high):
    width = low.shape[0]
    own_count = own.shape[0]
    parts = (
        (dense[:, width : width + own_count], own),
        (dense[:, :width], low),
        (dense[:, width + own_count :], high),
    )
    total = None
    for coeffs, field in parts:
        product = jnp.einsum(
            "ijrc,jcm->irm",
            coeffs,
            field,
            precision=HIGHEST,
            preferred_element_type=jnp.float32,
        )
        total = product if total is None else total + product
    regrouped = lax.all_to_all(total, "mode", split_axis=2, concat_axis=1, tiled=True)
    return regrouped.reshape(-1, regrouped.shape[2])


def staged(vectors, force_blocks, inverse_blocks, neighbours):
    row_count, col_count = vectors.shape
    block_size = inverse_blocks.shape[1]
    block_rows = row_count // block_size
    slab_count = lax.axis_size("space")
    total_rows = row_count * slab_count
    own_layers = block_rows // CELLS
    layer_total = own_layers * slab_count
    slab_index = lax.axis_index("space")
    mode_index = lax.axis_index("mode")
    layer_of = neighbours // CELLS
    relative = (layer_of - slab_index * own_layers + 1) % layer_total
    local_ids = relative * CELLS + neighbours % CELLS
    ext_blocks = block_rows + 2 * CELLS
    dense = dense_rows(force_blocks, local_ids, ext_blocks)

    stacked_x = vectors.reshape(block_rows, block_size, col_count)
    full_x = lax.all_gather(stacked_x, "mode", axis=2, tiled=True)
    low_x, high_x = halo(full_x, CELLS)
    image_x = apply_dense(dense, low_x, full_x, high_x)
    mode_count = full_x.shape[2]
    flat_x = full_x.reshape(row_count, mode_count)
    rayleigh = (
        space_sum(
            jnp.einsum(
                "ra,rj->aj",
                flat_x,
                image_x,
                precision=HIGHEST,
                preferred_element_type=jnp.float32,
            )
        )
        / total_rows
    )
    residual = image_x - jnp.dot(
        flat_x, rayleigh, precision=HIGHEST, preferred_element_type=jnp.float32
    )
    search_raw = jnp.einsum(
        "brc,bcm->brm",
        inverse_blocks,
        residual.reshape(block_rows, block_size, col_count),
        precision=HIGHEST,
        preferred_element_type=jnp.float32,
    )
    full_s = lax.all_gather(search_raw, "mode", axis=2, tiled=True)
    flat_s = full_s.reshape(row_count, mode_count)
    own_s = search_raw.reshape(row_count, col_count)

    squares = jnp.sum(flat_s * flat_s, axis=0)
    cross = jnp.einsum(
        "ra,rgj->agj",
        flat_s,
        jnp.stack([vectors, own_s, image_x], axis=1),
        precision=HIGHEST,
        preferred_element_type=jnp.float32,
    )
    x_s = jnp.einsum(
        "ra,rgj->agj",
        flat_x,
        jnp.stack([vectors, own_s], axis=1),
        precision=HIGHEST,
        preferred_element_type=jnp.float32,
    )
    packed = jnp.concatenate([cross.reshape(-1), x_s.reshape(-1), squares])
    summed = space_sum(packed)
    cross_sum = summed[: cross.size].reshape(cross.shape)
    x_s_sum = summed[cross.size : cross.size + x_s.size].reshape(x_s.shape)
    scales_all = lax.rsqrt(summed[cross.size + x_s.size :] / total_rows + 1e-06)
    scales_own = lax.dynamic_slice_in_dim(scales_all, mode_index * col_count, col_count)

    low_s, high_s = halo(full_s, CELLS)
    image_s = apply_dense(dense, low_s, full_s, high_s)
    basis = jnp.concatenate([flat_x, flat_s], axis=1)
    last = space_sum(
        jnp.einsum(
            "ra,rj->aj", basis, image_s, precision=HIGHEST, preferred_element_type=jnp.float32
        )
    )

    w_block = own_s * scales_own
    hw_block = image_s * scales_own
    col = scales_own[None, :]
    row = scales_all[:, None]
    gram_b = jnp.concatenate(
        [
            jnp.stack([x_s_sum[:, 0], x_s_sum[:, 1] * col], axis=1) / total_rows,
            jnp.stack([cross_sum[:, 0] * row, cross_sum[:, 1] * row * col], axis=1) / total_rows,
        ],
        axis=0,
    )
    gram_a = jnp.concatenate(
        [
            jnp.stack([rayleigh, last[:mode_count] * col / total_rows], axis=1),
            jnp.stack([cross_sum[:, 2] * row, last[mode_count:] * row * col], axis=1) / total_rows,
        ],
        axis=0,
    )
    return (w_block, hw_block, gram_a, gram_b)


def solution(mesh):
    in_specs = (
        P("space", "mode"),
        P("space", None, "mode", None),
        P("space", None, None),
        P("space", None),
    )
    out_specs = (
        P("space", "mode"),
        P("space", "mode"),
        P(None, None, "mode"),
        P(None, None, "mode"),
    )
    return jax.shard_map(staged, mesh=mesh, in_specs=in_specs, out_specs=out_specs, check_vma=False)
```

```python
import jax
import jax.numpy as jnp
from jax import lax
from jax.sharding import PartitionSpec as P


CELLS = 9
HIGHEST = lax.Precision.HIGHEST


def space_sum(value):
    count = lax.axis_size("space")
    step = 1
    while step < count:
        pairs = [(i, i ^ step) for i in range(count)]
        value = value + lax.ppermute(value, "space", pairs)
        step *= 2
    return value


def halo(block, width):
    count = lax.axis_size("space")
    forward = [(i, (i + 1) % count) for i in range(count)]
    backward = [((i + 1) % count, i) for i in range(count)]
    mode_count = lax.axis_size("mode")
    core = lax.axis_index("mode") % 2
    half = block.shape[2] // 2
    siblings = [(i, i ^ 1) for i in range(mode_count)]

    def send(piece, pairs):
        mine = lax.dynamic_slice_in_dim(piece, core * half, half, axis=2)
        got = lax.ppermute(mine, "space", pairs)
        other = lax.ppermute(got, "mode", siblings)
        return jnp.where(
            core == 0,
            jnp.concatenate([got, other], axis=2),
            jnp.concatenate([other, got], axis=2),
        )

    low = send(block[block.shape[0] - width :], forward)
    high = send(block[:width], backward)
    return low, high


def dense_rows(force_blocks, local_ids, ext_blocks):
    block_rows, neigh = local_ids.shape
    columns = jnp.arange(ext_blocks, dtype=jnp.int32)
    onehot = local_ids[:, :, None] == columns[None, None, :]
    offsets = jnp.arange(neigh, dtype=jnp.int32)
    which = jnp.sum(jnp.where(onehot, offsets[None, :, None], 0), axis=1)
    valid = jnp.any(onehot, axis=1)
    picked = force_blocks[jnp.arange(block_rows, dtype=jnp.int32)[:, None], which]
    return jnp.where(valid[:, :, None, None], picked, 0.0)


def apply_dense(dense, low, own, high):
    width = low.shape[0]
    own_count = own.shape[0]
    parts = (
        (dense[:, width : width + own_count], own),
        (dense[:, :width], low),
        (dense[:, width + own_count :], high),
    )
    total = None
    for coeffs, field in parts:
        product = jnp.einsum(
            "ijrc,jcm->irm",
            coeffs,
            field,
            precision=HIGHEST,
            preferred_element_type=jnp.float32,
        )
        total = product if total is None else total + product
    mode_count = lax.axis_size("mode")
    me = lax.axis_index("mode")
    _, _, modes = total.shape
    width = modes // mode_count
    pieces = []
    for shift in range(mode_count):
        target = (me + shift) % mode_count
        piece = lax.dynamic_slice_in_dim(total, target * width, width, axis=2)
        if shift:
            pairs = [(i, (i + shift) % mode_count) for i in range(mode_count)]
            piece = lax.ppermute(piece, "mode", pairs)
        pieces.append(piece)
    stacked = jnp.stack(pieces)
    order = (me - jnp.arange(mode_count, dtype=jnp.int32)) % mode_count
    by_source = jnp.take(stacked, order, axis=0)
    return jnp.transpose(by_source, (1, 0, 2, 3)).reshape(-1, width)


def staged(vectors, force_blocks, inverse_blocks, neighbours):
    row_count, col_count = vectors.shape
    block_size = inverse_blocks.shape[1]
    block_rows = row_count // block_size
    slab_count = lax.axis_size("space")
    total_rows = row_count * slab_count
    own_layers = block_rows // CELLS
    layer_total = own_layers * slab_count
    slab_index = lax.axis_index("space")
    mode_index = lax.axis_index("mode")
    layer_of = neighbours // CELLS
    relative = (layer_of - slab_index * own_layers + 1) % layer_total
    local_ids = relative * CELLS + neighbours % CELLS
    ext_blocks = block_rows + 2 * CELLS
    dense = dense_rows(force_blocks, local_ids, ext_blocks)

    stacked_x = vectors.reshape(block_rows, block_size, col_count)
    full_x = lax.all_gather(stacked_x, "mode", axis=2, tiled=True)
    low_x, high_x = halo(full_x, CELLS)
    image_x = apply_dense(dense, low_x, full_x, high_x)
    mode_count = full_x.shape[2]
    flat_x = full_x.reshape(row_count, mode_count)
    rayleigh = (
        space_sum(
            jnp.einsum(
                "ra,rj->aj",
                flat_x,
                image_x,
                precision=HIGHEST,
                preferred_element_type=jnp.float32,
            )
        )
        / total_rows
    )
    residual = image_x - jnp.dot(
        flat_x, rayleigh, precision=HIGHEST, preferred_element_type=jnp.float32
    )
    search_raw = jnp.einsum(
        "brc,bcm->brm",
        inverse_blocks,
        residual.reshape(block_rows, block_size, col_count),
        precision=HIGHEST,
        preferred_element_type=jnp.float32,
    )
    full_s = lax.all_gather(search_raw, "mode", axis=2, tiled=True)
    flat_s = full_s.reshape(row_count, mode_count)
    own_s = search_raw.reshape(row_count, col_count)

    squares = jnp.sum(flat_s * flat_s, axis=0)
    cross = jnp.einsum(
        "ra,rgj->agj",
        flat_s,
        jnp.stack([vectors, own_s, image_x], axis=1),
        precision=HIGHEST,
        preferred_element_type=jnp.float32,
    )
    x_s = jnp.einsum(
        "ra,rgj->agj",
        flat_x,
        jnp.stack([vectors, own_s], axis=1),
        precision=HIGHEST,
        preferred_element_type=jnp.float32,
    )
    packed = jnp.concatenate([cross.reshape(-1), x_s.reshape(-1), squares])
    summed = space_sum(packed)
    cross_sum = summed[: cross.size].reshape(cross.shape)
    x_s_sum = summed[cross.size : cross.size + x_s.size].reshape(x_s.shape)
    scales_all = lax.rsqrt(summed[cross.size + x_s.size :] / total_rows + 1e-06)
    scales_own = lax.dynamic_slice_in_dim(scales_all, mode_index * col_count, col_count)

    low_s, high_s = halo(full_s, CELLS)
    image_s = apply_dense(dense, low_s, full_s, high_s)
    basis = jnp.concatenate([flat_x, flat_s], axis=1)
    last = space_sum(
        jnp.einsum(
            "ra,rj->aj", basis, image_s, precision=HIGHEST, preferred_element_type=jnp.float32
        )
    )

    w_block = own_s * scales_own
    hw_block = image_s * scales_own
    col = scales_own[None, :]
    row = scales_all[:, None]
    gram_b = jnp.concatenate(
        [
            jnp.stack([x_s_sum[:, 0], x_s_sum[:, 1] * col], axis=1) / total_rows,
            jnp.stack([cross_sum[:, 0] * row, cross_sum[:, 1] * row * col], axis=1) / total_rows,
        ],
        axis=0,
    )
    gram_a = jnp.concatenate(
        [
            jnp.stack([rayleigh, last[:mode_count] * col / total_rows], axis=1),
            jnp.stack([cross_sum[:, 2] * row, last[mode_count:] * row * col], axis=1) / total_rows,
        ],
        axis=0,
    )
    return (w_block, hw_block, gram_a, gram_b)


def solution(mesh):
    in_specs = (
        P("space", "mode"),
        P("space", None, "mode", None),
        P("space", None, None),
        P("space", None),
    )
    out_specs = (
        P("space", "mode"),
        P("space", "mode"),
        P(None, None, "mode"),
        P(None, None, "mode"),
    )
    return jax.shard_map(staged, mesh=mesh, in_specs=in_specs, out_specs=out_specs, check_vma=False)
```

```python
import jax
import jax.numpy as jnp
from jax import lax
from jax.sharding import PartitionSpec as P


CELLS = 9
HIGHEST = lax.Precision.HIGHEST


def space_sum(value):
    count = lax.axis_size("space")
    step = 1
    while step < count:
        pairs = [(i, i ^ step) for i in range(count)]
        value = value + lax.ppermute(value, "space", pairs)
        step *= 2
    return value


def halo(block, width):
    count = lax.axis_size("space")
    forward = [(i, (i + 1) % count) for i in range(count)]
    backward = [((i + 1) % count, i) for i in range(count)]
    mode_count = lax.axis_size("mode")
    core = lax.axis_index("mode") % 2
    half = block.shape[2] // 2
    siblings = [(i, i ^ 1) for i in range(mode_count)]

    def send(piece, pairs):
        mine = lax.dynamic_slice_in_dim(piece, core * half, half, axis=2)
        got = lax.ppermute(mine, "space", pairs)
        other = lax.ppermute(got, "mode", siblings)
        return jnp.where(
            core == 0,
            jnp.concatenate([got, other], axis=2),
            jnp.concatenate([other, got], axis=2),
        )

    low = send(block[block.shape[0] - width :], forward)
    high = send(block[:width], backward)
    return low, high


def dense_rows(force_blocks, local_ids, ext_blocks):
    block_rows, neigh = local_ids.shape
    columns = jnp.arange(ext_blocks, dtype=jnp.int32)
    onehot = local_ids[:, :, None] == columns[None, None, :]
    offsets = jnp.arange(neigh, dtype=jnp.int32)
    which = jnp.sum(jnp.where(onehot, offsets[None, :, None], 0), axis=1)
    valid = jnp.any(onehot, axis=1)
    picked = force_blocks[jnp.arange(block_rows, dtype=jnp.int32)[:, None], which]
    return jnp.where(valid[:, :, None, None], picked, 0.0)


def apply_dense(dense, low, own, high):
    width = low.shape[0]
    own_count = own.shape[0]
    parts = (
        (dense[:, width : width + own_count], own),
        (dense[:, :width], low),
        (dense[:, width + own_count :], high),
    )
    total = None
    for coeffs, field in parts:
        product = jnp.einsum(
            "ijrc,jcm->irm",
            coeffs,
            field,
            precision=HIGHEST,
            preferred_element_type=jnp.float32,
        )
        total = product if total is None else total + product
    mode_count = lax.axis_size("mode")
    me = lax.axis_index("mode")
    block_rows, rows, modes = total.shape
    width = modes // mode_count
    slots = jnp.transpose(total.reshape(block_rows, rows, mode_count, width), (2, 0, 1, 3))
    slot_ids = jnp.arange(mode_count, dtype=jnp.int32)
    bit = 1
    while bit < mode_count:
        pairs = [(i, i ^ bit) for i in range(mode_count)]
        received = lax.ppermute(slots, "mode", pairs)
        swapped = received[jnp.array([k ^ bit for k in range(mode_count)])]
        take = (slot_ids & bit) != (me & bit)
        slots = jnp.where(take[:, None, None, None], swapped, slots)
        bit *= 2
    return jnp.transpose(slots, (1, 0, 2, 3)).reshape(-1, width)


def staged(vectors, force_blocks, inverse_blocks, neighbours):
    row_count, col_count = vectors.shape
    block_size = inverse_blocks.shape[1]
    block_rows = row_count // block_size
    slab_count = lax.axis_size("space")
    total_rows = row_count * slab_count
    own_layers = block_rows // CELLS
    layer_total = own_layers * slab_count
    slab_index = lax.axis_index("space")
    mode_index = lax.axis_index("mode")
    layer_of = neighbours // CELLS
    relative = (layer_of - slab_index * own_layers + 1) % layer_total
    local_ids = relative * CELLS + neighbours % CELLS
    ext_blocks = block_rows + 2 * CELLS
    dense = dense_rows(force_blocks, local_ids, ext_blocks)

    stacked_x = vectors.reshape(block_rows, block_size, col_count)
    full_x = lax.all_gather(stacked_x, "mode", axis=2, tiled=True)
    low_x, high_x = halo(full_x, CELLS)
    image_x = apply_dense(dense, low_x, full_x, high_x)
    mode_count = full_x.shape[2]
    flat_x = full_x.reshape(row_count, mode_count)
    rayleigh = (
        space_sum(
            jnp.einsum(
                "ra,rj->aj",
                flat_x,
                image_x,
                precision=HIGHEST,
                preferred_element_type=jnp.float32,
            )
        )
        / total_rows
    )
    residual = image_x - jnp.dot(
        flat_x, rayleigh, precision=HIGHEST, preferred_element_type=jnp.float32
    )
    search_raw = jnp.einsum(
        "brc,bcm->brm",
        inverse_blocks,
        residual.reshape(block_rows, block_size, col_count),
        precision=HIGHEST,
        preferred_element_type=jnp.float32,
    )
    full_s = lax.all_gather(search_raw, "mode", axis=2, tiled=True)
    flat_s = full_s.reshape(row_count, mode_count)
    own_s = search_raw.reshape(row_count, col_count)

    squares = jnp.sum(flat_s * flat_s, axis=0)
    cross = jnp.einsum(
        "ra,rgj->agj",
        flat_s,
        jnp.stack([vectors, own_s, image_x], axis=1),
        precision=HIGHEST,
        preferred_element_type=jnp.float32,
    )
    x_s = jnp.einsum(
        "ra,rgj->agj",
        flat_x,
        jnp.stack([vectors, own_s], axis=1),
        precision=HIGHEST,
        preferred_element_type=jnp.float32,
    )
    packed = jnp.concatenate([cross.reshape(-1), x_s.reshape(-1), squares])
    summed = space_sum(packed)
    cross_sum = summed[: cross.size].reshape(cross.shape)
    x_s_sum = summed[cross.size : cross.size + x_s.size].reshape(x_s.shape)
    scales_all = lax.rsqrt(summed[cross.size + x_s.size :] / total_rows + 1e-06)
    scales_own = lax.dynamic_slice_in_dim(scales_all, mode_index * col_count, col_count)

    low_s, high_s = halo(full_s, CELLS)
    image_s = apply_dense(dense, low_s, full_s, high_s)
    basis = jnp.concatenate([flat_x, flat_s], axis=1)
    last = space_sum(
        jnp.einsum(
            "ra,rj->aj", basis, image_s, precision=HIGHEST, preferred_element_type=jnp.float32
        )
    )

    w_block = own_s * scales_own
    hw_block = image_s * scales_own
    col = scales_own[None, :]
    row = scales_all[:, None]
    gram_b = jnp.concatenate(
        [
            jnp.stack([x_s_sum[:, 0], x_s_sum[:, 1] * col], axis=1) / total_rows,
            jnp.stack([cross_sum[:, 0] * row, cross_sum[:, 1] * row * col], axis=1) / total_rows,
        ],
        axis=0,
    )
    gram_a = jnp.concatenate(
        [
            jnp.stack([rayleigh, last[:mode_count] * col / total_rows], axis=1),
            jnp.stack([cross_sum[:, 2] * row, last[mode_count:] * row * col], axis=1) / total_rows,
        ],
        axis=0,
    )
    return (w_block, hw_block, gram_a, gram_b)


def solution(mesh):
    in_specs = (
        P("space", "mode"),
        P("space", None, "mode", None),
        P("space", None, None),
        P("space", None),
    )
    out_specs = (
        P("space", "mode"),
        P("space", "mode"),
        P(None, None, "mode"),
        P(None, None, "mode"),
    )
    return jax.shard_map(staged, mesh=mesh, in_specs=in_specs, out_specs=out_specs, check_vma=False)
```

```python
import jax
import jax.numpy as jnp
from jax import lax
from jax.sharding import PartitionSpec as P


CELLS = 9
HIGHEST = lax.Precision.HIGHEST


def space_sum(value):
    count = lax.axis_size("space")
    step = 1
    while step < count:
        pairs = [(i, i ^ step) for i in range(count)]
        value = value + lax.ppermute(value, "space", pairs)
        step *= 2
    return value


def halo(block, width):
    count = lax.axis_size("space")
    forward = [(i, (i + 1) % count) for i in range(count)]
    backward = [((i + 1) % count, i) for i in range(count)]
    mode_count = lax.axis_size("mode")
    core = lax.axis_index("mode") % 2
    half = block.shape[2] // 2
    siblings = [(i, i ^ 1) for i in range(mode_count)]

    def send(piece, pairs):
        mine = lax.dynamic_slice_in_dim(piece, core * half, half, axis=2)
        got = lax.ppermute(mine, "space", pairs)
        other = lax.ppermute(got, "mode", siblings)
        return jnp.where(
            core == 0,
            jnp.concatenate([got, other], axis=2),
            jnp.concatenate([other, got], axis=2),
        )

    low = send(block[block.shape[0] - width :], forward)
    high = send(block[:width], backward)
    return low, high


def dense_rows(force_blocks, local_ids, ext_blocks):
    block_rows, neigh = local_ids.shape
    columns = jnp.arange(ext_blocks, dtype=jnp.int32)
    onehot = local_ids[:, :, None] == columns[None, None, :]
    offsets = jnp.arange(neigh, dtype=jnp.int32)
    which = jnp.sum(jnp.where(onehot, offsets[None, :, None], 0), axis=1)
    valid = jnp.any(onehot, axis=1)
    picked = force_blocks[jnp.arange(block_rows, dtype=jnp.int32)[:, None], which]
    return jnp.where(valid[:, :, None, None], picked, 0.0)


def apply_dense(dense, low, own, high):
    width = low.shape[0]
    own_count = own.shape[0]
    parts = (
        (dense[:, width : width + own_count], own),
        (dense[:, :width], low),
        (dense[:, width + own_count :], high),
    )
    total = None
    for coeffs, field in parts:
        product = jnp.einsum(
            "ijrc,jcm->irm",
            coeffs,
            field,
            precision=HIGHEST,
            preferred_element_type=jnp.float32,
        )
        total = product if total is None else total + product
    mode_count = lax.axis_size("mode")
    me = lax.axis_index("mode")
    _, _, modes = total.shape
    width = modes // mode_count
    pieces = []
    for shift in range(mode_count):
        target = (me + shift) % mode_count
        piece = lax.dynamic_slice_in_dim(total, target * width, width, axis=2)
        if shift:
            pairs = [(i, (i + shift) % mode_count) for i in range(mode_count)]
            piece = lax.ppermute(piece, "mode", pairs)
        pieces.append(piece)
    stacked = jnp.stack(pieces)
    order = (me - jnp.arange(mode_count, dtype=jnp.int32)) % mode_count
    by_source = jnp.take(stacked, order, axis=0)
    return jnp.transpose(by_source, (1, 0, 2, 3)).reshape(-1, width)


def staged(vectors, force_blocks, inverse_blocks, neighbours):
    row_count, col_count = vectors.shape
    block_size = inverse_blocks.shape[1]
    block_rows = row_count // block_size
    slab_count = lax.axis_size("space")
    total_rows = row_count * slab_count
    own_layers = block_rows // CELLS
    layer_total = own_layers * slab_count
    slab_index = lax.axis_index("space")
    mode_index = lax.axis_index("mode")
    layer_of = neighbours // CELLS
    relative = (layer_of - slab_index * own_layers + 1) % layer_total
    local_ids = relative * CELLS + neighbours % CELLS
    ext_blocks = block_rows + 2 * CELLS
    dense = dense_rows(force_blocks, local_ids, ext_blocks)

    stacked_x = vectors.reshape(block_rows, block_size, col_count)
    full_x = lax.all_gather(stacked_x, "mode", axis=2, tiled=True)
    low_x, high_x = halo(full_x, CELLS)
    image_x = apply_dense(dense, low_x, full_x, high_x)
    mode_count = full_x.shape[2]
    flat_x = full_x.reshape(row_count, mode_count)
    first = (
        space_sum(
            jnp.einsum(
                "ra,rgj->agj",
                flat_x,
                jnp.stack([image_x, vectors], axis=1),
                precision=HIGHEST,
                preferred_element_type=jnp.float32,
            )
        )
        / total_rows
    )
    rayleigh = first[:, 0]
    residual = image_x - jnp.dot(
        flat_x, rayleigh, precision=HIGHEST, preferred_element_type=jnp.float32
    )
    search_raw = jnp.einsum(
        "brc,bcm->brm",
        inverse_blocks,
        residual.reshape(block_rows, block_size, col_count),
        precision=HIGHEST,
        preferred_element_type=jnp.float32,
    )
    full_s = lax.all_gather(search_raw, "mode", axis=2, tiled=True)
    flat_s = full_s.reshape(row_count, mode_count)
    own_s = search_raw.reshape(row_count, col_count)

    squares = jnp.sum(flat_s * flat_s, axis=0)
    cross = jnp.einsum(
        "ra,rgj->agj",
        flat_s,
        jnp.stack([vectors, own_s, image_x], axis=1),
        precision=HIGHEST,
        preferred_element_type=jnp.float32,
    )
    x_s = jnp.einsum(
        "ra,rj->aj", flat_x, own_s, precision=HIGHEST, preferred_element_type=jnp.float32
    )
    packed = jnp.concatenate([cross.reshape(-1), x_s.reshape(-1), squares])
    summed = space_sum(packed)
    cross_sum = summed[: cross.size].reshape(cross.shape)
    x_s_sum = summed[cross.size : cross.size + x_s.size].reshape(x_s.shape)
    scales_all = lax.rsqrt(summed[cross.size + x_s.size :] / total_rows + 1e-06)
    scales_own = lax.dynamic_slice_in_dim(scales_all, mode_index * col_count, col_count)

    low_s, high_s = halo(full_s, CELLS)
    image_s = apply_dense(dense, low_s, full_s, high_s)
    basis = jnp.concatenate([flat_x, flat_s], axis=1)
    last = space_sum(
        jnp.einsum(
            "ra,rj->aj", basis, image_s, precision=HIGHEST, preferred_element_type=jnp.float32
        )
    )

    w_block = own_s * scales_own
    hw_block = image_s * scales_own
    col = scales_own[None, :]
    row = scales_all[:, None]
    gram_b = jnp.concatenate(
        [
            jnp.stack([first[:, 1], x_s_sum * col / total_rows], axis=1),
            jnp.stack([cross_sum[:, 0] * row, cross_sum[:, 1] * row * col], axis=1) / total_rows,
        ],
        axis=0,
    )
    gram_a = jnp.concatenate(
        [
            jnp.stack([rayleigh, last[:mode_count] * col / total_rows], axis=1),
            jnp.stack([cross_sum[:, 2] * row, last[mode_count:] * row * col], axis=1) / total_rows,
        ],
        axis=0,
    )
    return (w_block, hw_block, gram_a, gram_b)


def solution(mesh):
    in_specs = (
        P("space", "mode"),
        P("space", None, "mode", None),
        P("space", None, None),
        P("space", None),
    )
    out_specs = (
        P("space", "mode"),
        P("space", "mode"),
        P(None, None, "mode"),
        P(None, None, "mode"),
    )
    return jax.shard_map(staged, mesh=mesh, in_specs=in_specs, out_specs=out_specs, check_vma=False)
```
